512 devices in a mesh: seq: 128 (over x, z, core), grp: 4 (over y).
Axes of the slice: x: 4, y: 4, z: 16, core: 2. Of those that a mesh axis runs over, the one named last changes fastest.
Arguments:
- linear_query: bfloat16 [65536, 256], P(('grp', 'seq')), parts along dimension 0, may hold values from -6 to 6
- linear_key: bfloat16 [65536, 256], P(('grp', 'seq')), parts along dimension 0, may hold values from -16 to 16
- values: bfloat16 [65536, 2048], P(('grp', 'seq')), parts along dimension 0, may hold values from -6 to 6
- window_query: bfloat16 [65536, 2048], P(('grp', 'seq')), parts along dimension 0, may hold values from -5 to 5
- window_key: bfloat16 [65536, 2048], P(('grp', 'seq')), parts along dimension 0, may hold values from -5 to 5
Outputs:
- linear_out: float32 [65536, 2048], P(('grp', 'seq')), parts along dimension 0
- window_out: bfloat16 [65536, 2048], P(('grp', 'seq')), parts along dimension 0
The draws below stay inside these ranges and needn't reach their ends.
There are 4 independent parts, one for each index of `grp`. The reference program is written for one: setup_inputs(seed, part) draws one part's arguments, and reference() takes and returns one part's arrays. A program takes and returns all parts, laid end to end along the dimension named above; each array names one. Nothing has to cross between parts.
All inputs are finite; a program needn't handle non-finite values.
Results may differ from the reference program's by a relative error of at most 0.0085.
Values may be sent and summed in bfloat16 or wider, within the bound.
No kernel may reach another device: no remote copies, remote signals or barrier semaphores. Data moves between devices by JAX's collectives and lax.ppermute only.
A program may use at most 64 MiB of HBM per device.

```python
import math
import jax
import jax.numpy as jnp
from jax import lax

HEADS = 16
FEAT = 16
HEAD_DIM = 128
WINDOW = 256
TOKENS = 16384


def draw_linear_key(key, part):
    row_scale = jnp.exp(jax.random.uniform(jax.random.fold_in(key, 3), (TOKENS, 1), jnp.float32, math.log(0.35), math.log(3.5)))
    column_scale = jnp.exp(jax.random.uniform(jax.random.fold_in(key, 4), (1, HEADS * FEAT), jnp.float32, math.log(0.35), math.log(3.5)))
    sample = jax.random.normal(jax.random.fold_in(key, 5), (TOKENS, HEADS * FEAT), jnp.float32)
    return jnp.clip(sample * row_scale * column_scale, -16.0, 16.0).astype(jnp.bfloat16)


def draw_window_query(key, part):
    sample = jax.random.normal(jax.random.fold_in(key, 1), (TOKENS, HEADS * HEAD_DIM), jnp.float32)
    return jnp.clip(sample, -5.0, 5.0).astype(jnp.bfloat16)


def draw_window_key(key, part):
    row_scale = jnp.exp(jax.random.uniform(jax.random.fold_in(key, 6), (TOKENS, 1), jnp.float32, math.log(0.3), math.log(3.0)))
    sample = row_scale * jax.random.normal(jax.random.fold_in(key, 2), (TOKENS, HEADS * HEAD_DIM), jnp.float32)
    return jnp.clip(sample, -5.0, 5.0).astype(jnp.bfloat16)


def steps_of(key, extent, cuts, low, high):
    gain, own = 1.0, jax.random.fold_in(key, 6)
    for axis_at, parts in cuts:
        heights = jnp.exp(jax.random.uniform(jax.random.fold_in(own, axis_at), (parts,), jnp.float32, low / len(cuts), high / len(cuts)))
        gain = gain * jnp.repeat(heights, extent[axis_at] // parts).reshape([-1 if axis == axis_at else 1 for axis in range(len(extent))])
    return gain


def scatter_about(key, dims, spread, limit, pieces=(), held_as=jnp.bfloat16):
    gain = steps_of(key, dims, pieces, -0.22, 0.18) if pieces else 1.0
    values = jax.random.normal(key, dims, jnp.float32) * spread * gain
    return jnp.minimum(jnp.maximum(values, -limit), limit).astype(held_as)


def setup_inputs(seed: int = 0, part: int = 0) -> dict:
    key_list = jax.random.split(jax.random.key(seed), 6)
    part_splits = jax.random.split(jax.random.fold_in(key_list[5], part), 6)
    return {
        "linear_query": scatter_about(part_splits[0], (TOKENS, HEADS * FEAT), 1.0, 6.0, ((0, 128),)),
        "linear_key": draw_linear_key(jax.random.fold_in(jax.random.fold_in(key_list[5], part), 71), part),
        "values": scatter_about(part_splits[2], (TOKENS, HEADS * HEAD_DIM), 1.0, 6.0, ((0, 128),)),
        "window_query": draw_window_query(jax.random.fold_in(jax.random.fold_in(key_list[5], part), 71), part),
        "window_key": draw_window_key(jax.random.fold_in(jax.random.fold_in(key_list[5], part), 71), part),
    }


PRECISE = lax.Precision.HIGHEST
HALF_ROOT = 0.7071067811865476


def full_features(scaled):
    row_count, head_count, feat_count = scaled.shape
    columns = jnp.transpose(scaled, (1, 2, 0))
    outer_prod = (columns[:, :, None, :] * columns[:, None, :, :] * HALF_ROOT).reshape(head_count, feat_count * feat_count, row_count)
    return jnp.concatenate([jnp.ones((head_count, 1, row_count), jnp.float32), columns, outer_prod], axis=1)


def reference(linear_query, linear_key, values, window_query, window_key):
    token_count = values.shape[0]
    head_count = linear_query.shape[1] // FEAT
    value_width = values.shape[1] // head_count
    block_size = math.gcd(token_count, 512)
    block_count = token_count // block_size
    feat_total = 1 + FEAT + FEAT * FEAT
    query_scaled = (linear_query.astype(jnp.float32) * FEAT ** -0.25).reshape(block_count, block_size, head_count, FEAT)
    key_scaled = (linear_key.astype(jnp.float32) * FEAT ** -0.25).reshape(block_count, block_size, head_count, FEAT)
    value_heads = values.astype(jnp.float32).reshape(block_count, block_size, head_count, value_width)
    causal = jnp.arange(block_size)[:, None] >= jnp.arange(block_size)[None, :]

    def advance(running, block_data):
        state, normer = running
        query_block, key_block, value_block = block_data
        query_feats = full_features(query_block)
        key_feats = full_features(key_block)
        inner_prod = jnp.einsum("thf,jhf->htj", query_block, key_block, precision=PRECISE)
        kernel = jnp.where(causal[None], 1.0 + inner_prod + 0.5 * inner_prod * inner_prod, 0.0)
        numerator = jnp.einsum("htj,jhv->thv", kernel, value_block, precision=PRECISE) + jnp.einsum("hpt,hpv->thv", query_feats, state, precision=PRECISE)
        denominator = jnp.sum(kernel, axis=2).T + jnp.einsum("hpt,hp->th", query_feats, normer, precision=PRECISE)
        state = state + jnp.einsum("hpr,rhv->hpv", key_feats, value_block, precision=PRECISE)
        normer = normer + jnp.sum(key_feats, axis=2)
        return (state, normer), numerator / denominator[:, :, None]

    initial = (jnp.zeros((head_count, feat_total, value_width), jnp.float32), jnp.zeros((head_count, feat_total), jnp.float32))
    unused, blocks = lax.scan(advance, initial, (query_scaled, key_scaled, value_heads))
    linear_out = blocks.reshape(token_count, head_count * value_width)

    width = values.shape[1]
    pad_keys = jnp.concatenate([jnp.zeros((WINDOW, width), window_key.dtype), window_key], axis=0)
    pad_values = jnp.concatenate([jnp.zeros((WINDOW, width), values.dtype), values], axis=0)

    def attend(block_index):
        begin = (block_index * block_size).astype(jnp.int32)
        query_block = lax.dynamic_slice_in_dim(window_query, begin, block_size, 0).astype(jnp.float32)
        key_block = lax.dynamic_slice_in_dim(pad_keys, begin, block_size + WINDOW, 0).astype(jnp.float32)
        value_block = lax.dynamic_slice_in_dim(pad_values, begin, block_size + WINDOW, 0).astype(jnp.float32)
        query_pos = begin + jnp.arange(block_size, dtype=jnp.int32)
        key_pos = begin - WINDOW + jnp.arange(block_size + WINDOW, dtype=jnp.int32)
        allowed = (key_pos[None, :] <= query_pos[:, None]) & (key_pos[None, :] > query_pos[:, None] - WINDOW) & (key_pos[None, :] >= 0)
        scores = jnp.einsum("thd,jhd->htj", query_block.reshape(block_size, head_count, value_width), key_block.reshape(block_size + WINDOW, head_count, value_width)) * HEAD_DIM ** -0.5
        masked = jnp.where(allowed[None], scores, -jnp.inf)
        largest = jnp.max(masked, axis=2, keepdims=True)
        exponent = jnp.exp(masked - largest)
        weights = (exponent / jnp.sum(exponent, axis=2, keepdims=True)).astype(jnp.bfloat16)
        mixed = jnp.einsum("htj,jhv->thv", weights.astype(jnp.float32), value_block.reshape(block_size + WINDOW, head_count, value_width))
        return mixed.astype(jnp.bfloat16).reshape(block_size, width)

    window_blocks = lax.map(attend, jnp.arange(block_count, dtype=jnp.int32))
    window_out = window_blocks.reshape(token_count, width)
    return (linear_out, window_out)
```

```python
import jax
import jax.numpy as jnp
import numpy as np
from jax import lax
from jax.sharding import Mesh
from jax.sharding import PartitionSpec as P

FEAT = 16
WINDOW = 256


PRECISE = lax.Precision.HIGHEST
HALF_ROOT = 0.7071067811865476
ROWS = ("grp", "sx", "sz", "sc")


def passed_along(block, axis, distance):
    devices = range(lax.axis_size(axis))
    route = [(i - distance, i) for i in devices if i - distance in devices]
    return lax.ppermute(block, axis, route)


def seq_index_of():
    return (
        lax.axis_index("sx") * (lax.axis_size("sz") * lax.axis_size("sc"))
        + lax.axis_index("sz") * lax.axis_size("sc")
        + lax.axis_index("sc")
    )


def pair_features(scaled):
    row_count, head_count, feat_count = scaled.shape
    columns = jnp.transpose(scaled, (1, 2, 0))
    lower_index, upper_index = np.triu_indices(feat_count)
    identity = np.eye(feat_count, dtype=np.float32)
    pick_lower = jnp.asarray(identity[:, lower_index])
    pick_upper = jnp.asarray(identity[:, upper_index])
    pair_weight = jnp.asarray(
        np.where(lower_index == upper_index, HALF_ROOT, 1.0).astype(np.float32)
    )
    left_side = jnp.einsum("hfr,fp->hpr", columns, pick_lower, precision=PRECISE)
    right_side = jnp.einsum("hfr,fp->hpr", columns, pick_upper, precision=PRECISE)
    paired = left_side * right_side * pair_weight[None, :, None]
    return jnp.concatenate(
        [jnp.ones((head_count, 1, row_count), jnp.float32), columns, paired], axis=1
    )


def prefix_before(local):
    nz = lax.axis_size("sz")
    nx = lax.axis_size("sx")
    core = lax.axis_index("sc")
    size = local.size
    unit = 2 * nz * 128
    padded = -(-size // unit) * unit
    width = padded // (2 * nz)
    flat = jnp.pad(local.reshape(-1), (0, padded - size)).reshape(2, nz, width)
    sent = jnp.where(core == 0, flat[1], flat[0])
    other = lax.ppermute(sent, "sc", [(0, 1), (1, 0)])
    mine = jnp.where(core == 0, flat[0], flat[1])
    chip_half = mine + other
    gathered = lax.all_to_all(chip_half, "sz", 0, 0, tiled=True)
    running = jnp.cumsum(gathered, axis=0)
    line_total = running[nz - 1]
    before_chip = running - gathered
    totals = lax.all_gather(line_total, "sx", axis=0, tiled=False)
    earlier_line = (jnp.arange(nx) < lax.axis_index("sx"))[:, None]
    line_offset = jnp.sum(jnp.where(earlier_line, totals, 0.0), axis=0)
    before_chip = before_chip + line_offset[None, :]
    chip_prefix = lax.all_to_all(before_chip, "sz", 0, 0, tiled=True)
    first_core = jnp.where(core == 0, flat[0], other)
    with_first = chip_prefix + first_core
    keep = jnp.where(core == 0, chip_prefix, with_first)
    give = jnp.where(core == 0, with_first, chip_prefix)
    got = lax.ppermute(give, "sc", [(0, 1), (1, 0)])
    halves = jnp.where(core == 0, jnp.stack([keep, got]), jnp.stack([got, keep]))
    return halves.reshape(-1)[:size].reshape(local.shape)


def on_device(linear_query, linear_key, values, window_query, window_key):
    row_count = values.shape[0]
    head_count = linear_query.shape[1] // FEAT
    value_width = values.shape[1] // head_count
    seq_index = seq_index_of()
    start_pos = seq_index * row_count
    query_scaled = (linear_query.astype(jnp.float32) * FEAT ** (-0.25)).reshape(
        row_count, head_count, FEAT
    )
    key_scaled = (linear_key.astype(jnp.float32) * FEAT ** (-0.25)).reshape(
        row_count, head_count, FEAT
    )
    value_heads = values.astype(jnp.float32).reshape(row_count, head_count, value_width)
    query_feats = pair_features(query_scaled)
    key_feats = pair_features(key_scaled)
    local_state = jnp.einsum("hpr,rhv->hpv", key_feats, value_heads, precision=PRECISE)
    local_norm = jnp.sum(key_feats, axis=2)
    local = jnp.concatenate([local_state, local_norm[:, :, None]], axis=2)
    prior = prefix_before(local)
    prior_state = prior[:, :, :value_width]
    prior_norm = prior[:, :, value_width]
    causal = jnp.arange(row_count)[:, None] >= jnp.arange(row_count)[None, :]
    inner_prod = jnp.einsum("thf,jhf->htj", query_scaled, key_scaled, precision=PRECISE)
    kernel = jnp.where(causal[None], 1.0 + inner_prod + 0.5 * inner_prod * inner_prod, 0.0)
    numerator = jnp.einsum("htj,jhv->thv", kernel, value_heads, precision=PRECISE) + jnp.einsum(
        "hpt,hpv->thv", query_feats, prior_state, precision=PRECISE
    )
    denominator = jnp.sum(kernel, axis=2).T + jnp.einsum(
        "hpt,hp->th", query_feats, prior_norm, precision=PRECISE
    )
    linear_out = (numerator / denominator[:, :, None]).reshape(row_count, head_count * value_width)
    seq_count = lax.axis_size("sx") * lax.axis_size("sz") * lax.axis_size("sc")
    span_rows = min(row_count, WINDOW)
    reach_count = -(-WINDOW // row_count)
    moved_keys = []
    moved_values = []
    flat_axes = ("sx", "sz", "sc")
    for distance in range(1, reach_count + 1):
        route = [(i - distance, i) for i in range(seq_count) if i - distance >= 0]
        arrived = lax.ppermute((window_key, values), flat_axes, route)
        moved_keys.append(arrived[0])
        moved_values.append(arrived[1])
    all_keys = jnp.concatenate(moved_keys[::-1] + [window_key], axis=0)
    all_values = jnp.concatenate(moved_values[::-1] + [values], axis=0)
    key_count = all_keys.shape[0]
    query_pos = start_pos + jnp.arange(row_count, dtype=jnp.int32)
    key_pos = start_pos - reach_count * span_rows + jnp.arange(key_count, dtype=jnp.int32)
    allowed = (
        (key_pos[None, :] <= query_pos[:, None])
        & (key_pos[None, :] > query_pos[:, None] - WINDOW)
        & (key_pos[None, :] >= 0)
    )
    scores = jnp.einsum(
        "thd,jhd->htj",
        window_query.reshape(row_count, head_count, value_width),
        all_keys.reshape(key_count, head_count, value_width),
        preferred_element_type=jnp.float32,
    ) * value_width ** (-0.5)
    masked = jnp.where(allowed[None], scores, -jnp.inf)
    largest = jnp.max(masked, axis=2, keepdims=True)
    exponent = jnp.exp(masked - largest)
    weights = (exponent / jnp.sum(exponent, axis=2, keepdims=True)).astype(jnp.bfloat16)
    mixed = jnp.einsum(
        "htj,jhv->thv",
        weights,
        all_values.reshape(key_count, head_count, value_width),
        preferred_element_type=jnp.float32,
    )
    window_out = mixed.astype(jnp.bfloat16).reshape(row_count, head_count * value_width)
    return (linear_out, window_out)


def split_seq(mesh):
    seq_devices = np.moveaxis(mesh.devices, mesh.axis_names.index("seq"), 0)[:, 0]
    seq_count = len(seq_devices)
    try:
        chips = sorted({tuple(d.coords) for d in seq_devices})
        cores = seq_count // len(chips)
        xs = sorted({c[0] for c in chips})
        nx = len(xs)
    except (AttributeError, TypeError):
        cores, nx = 2, max(1, seq_count // 32)
    nz = seq_count // (nx * cores)
    return nx, nz, cores


def solution(mesh):
    nx, nz, nc = split_seq(mesh)
    parts = {"seq": ((nx, nz, nc), ("sx", "sz", "sc")), "grp": ((mesh.shape["grp"],), ("grp",))}
    shape = sum((parts[name][0] for name in mesh.axis_names), ())
    names = sum((parts[name][1] for name in mesh.axis_names), ())
    inner = Mesh(mesh.devices.reshape(shape), names)
    return jax.shard_map(
        on_device,
        mesh=inner,
        in_specs=(P(ROWS, None),) * 5,
        out_specs=(P(ROWS, None), P(ROWS, None)),
        check_vma=False,
    )
```

```python
import jax
import jax.numpy as jnp
import numpy as np
from jax import lax
from jax.sharding import Mesh
from jax.sharding import PartitionSpec as P

FEAT = 16
WINDOW = 256


PRECISE = lax.Precision.HIGHEST
HALF_ROOT = 0.7071067811865476
ROWS = ("grp", "sx", "sz", "sc")


def passed_along(block, axis, distance):
    devices = range(lax.axis_size(axis))
    route = [(i - distance, i) for i in devices if i - distance in devices]
    return lax.ppermute(block, axis, route)


def seq_index_of():
    return (
        lax.axis_index("sx") * (lax.axis_size("sz") * lax.axis_size("sc"))
        + lax.axis_index("sz") * lax.axis_size("sc")
        + lax.axis_index("sc")
    )


def pair_features(scaled):
    row_count, head_count, feat_count = scaled.shape
    columns = jnp.transpose(scaled, (1, 2, 0))
    lower_index, upper_index = np.triu_indices(feat_count)
    identity = np.eye(feat_count, dtype=np.float32)
    pick_lower = jnp.asarray(identity[:, lower_index])
    pick_upper = jnp.asarray(identity[:, upper_index])
    pair_weight = jnp.asarray(
        np.where(lower_index == upper_index, HALF_ROOT, 1.0).astype(np.float32)
    )
    left_side = jnp.einsum("hfr,fp->hpr", columns, pick_lower, precision=PRECISE)
    right_side = jnp.einsum("hfr,fp->hpr", columns, pick_upper, precision=PRECISE)
    paired = left_side * right_side * pair_weight[None, :, None]
    return jnp.concatenate(
        [jnp.ones((head_count, 1, row_count), jnp.float32), columns, paired], axis=1
    )


def prefix_before(local):
    chips = lax.axis_size("sx") * lax.axis_size("sz")
    core = lax.axis_index("sc")
    size = local.size
    unit = 2 * chips * 128
    padded = -(-size // unit) * unit
    width = padded // (2 * chips)
    flat = jnp.pad(local.reshape(-1), (0, padded - size)).reshape(2, chips, width)
    sent = jnp.where(core == 0, flat[1], flat[0])
    other = lax.ppermute(sent, "sc", [(0, 1), (1, 0)])
    mine = jnp.where(core == 0, flat[0], flat[1])
    chip_half = mine + other
    gathered = lax.all_to_all(chip_half, ("sx", "sz"), 0, 0, tiled=True)
    before_chip = jnp.cumsum(gathered, axis=0) - gathered
    chip_prefix = lax.all_to_all(before_chip, ("sx", "sz"), 0, 0, tiled=True)
    first_core = jnp.where(core == 0, flat[0], other)
    with_first = chip_prefix + first_core
    keep = jnp.where(core == 0, chip_prefix, with_first)
    give = jnp.where(core == 0, with_first, chip_prefix)
    got = lax.ppermute(give, "sc", [(0, 1), (1, 0)])
    halves = jnp.where(core == 0, jnp.stack([keep, got]), jnp.stack([got, keep]))
    return halves.reshape(-1)[:size].reshape(local.shape)


def on_device(linear_query, linear_key, values, window_query, window_key):
    row_count = values.shape[0]
    head_count = linear_query.shape[1] // FEAT
    value_width = values.shape[1] // head_count
    seq_index = seq_index_of()
    start_pos = seq_index * row_count
    query_scaled = (linear_query.astype(jnp.float32) * FEAT ** (-0.25)).reshape(
        row_count, head_count, FEAT
    )
    key_scaled = (linear_key.astype(jnp.float32) * FEAT ** (-0.25)).reshape(
        row_count, head_count, FEAT
    )
    value_heads = values.astype(jnp.float32).reshape(row_count, head_count, value_width)
    query_feats = pair_features(query_scaled)
    key_feats = pair_features(key_scaled)
    local_state = jnp.einsum("hpr,rhv->hpv", key_feats, value_heads, precision=PRECISE)
    local_norm = jnp.sum(key_feats, axis=2)
    local = jnp.concatenate([local_state, local_norm[:, :, None]], axis=2)
    prior = prefix_before(local)
    prior_state = prior[:, :, :value_width]
    prior_norm = prior[:, :, value_width]
    causal = jnp.arange(row_count)[:, None] >= jnp.arange(row_count)[None, :]
    inner_prod = jnp.einsum("thf,jhf->htj", query_scaled, key_scaled, precision=PRECISE)
    kernel = jnp.where(causal[None], 1.0 + inner_prod + 0.5 * inner_prod * inner_prod, 0.0)
    numerator = jnp.einsum("htj,jhv->thv", kernel, value_heads, precision=PRECISE) + jnp.einsum(
        "hpt,hpv->thv", query_feats, prior_state, precision=PRECISE
    )
    denominator = jnp.sum(kernel, axis=2).T + jnp.einsum(
        "hpt,hp->th", query_feats, prior_norm, precision=PRECISE
    )
    linear_out = (numerator / denominator[:, :, None]).reshape(row_count, head_count * value_width)
    seq_count = lax.axis_size("sx") * lax.axis_size("sz") * lax.axis_size("sc")
    span_rows = row_count
    reach_count = 2
    assert reach_count * row_count >= WINDOW
    flat_axes = ("sx", "sz", "sc")
    core = lax.axis_index("sc")
    route = [(i - 2, i) for i in range(2, seq_count)]
    far = lax.ppermute((window_key, values), flat_axes, route)
    near = lax.ppermute(
        jax.tree.map(lambda o, f: jnp.where(core == 0, o, f), (window_key, values), far),
        "sc",
        [(0, 1), (1, 0)],
    )
    moved_keys = [near[0], far[0]]
    moved_values = [near[1], far[1]]
    all_keys = jnp.concatenate(moved_keys[::-1] + [window_key], axis=0)
    all_values = jnp.concatenate(moved_values[::-1] + [values], axis=0)
    key_count = all_keys.shape[0]
    query_pos = start_pos + jnp.arange(row_count, dtype=jnp.int32)
    key_pos = start_pos - reach_count * span_rows + jnp.arange(key_count, dtype=jnp.int32)
    allowed = (
        (key_pos[None, :] <= query_pos[:, None])
        & (key_pos[None, :] > query_pos[:, None] - WINDOW)
        & (key_pos[None, :] >= 0)
    )
    scores = jnp.einsum(
        "thd,jhd->htj",
        window_query.reshape(row_count, head_count, value_width),
        all_keys.reshape(key_count, head_count, value_width),
        preferred_element_type=jnp.float32,
    ) * value_width ** (-0.5)
    masked = jnp.where(allowed[None], scores, -jnp.inf)
    largest = jnp.max(masked, axis=2, keepdims=True)
    exponent = jnp.exp(masked - largest)
    weights = (exponent / jnp.sum(exponent, axis=2, keepdims=True)).astype(jnp.bfloat16)
    mixed = jnp.einsum(
        "htj,jhv->thv",
        weights,
        all_values.reshape(key_count, head_count, value_width),
        preferred_element_type=jnp.float32,
    )
    window_out = mixed.astype(jnp.bfloat16).reshape(row_count, head_count * value_width)
    return (linear_out, window_out)


def split_seq(mesh):
    seq_devices = np.moveaxis(mesh.devices, mesh.axis_names.index("seq"), 0)[:, 0]
    seq_count = len(seq_devices)
    try:
        chips = sorted({tuple(d.coords) for d in seq_devices})
        cores = seq_count // len(chips)
        xs = sorted({c[0] for c in chips})
        nx = len(xs)
    except (AttributeError, TypeError):
        cores, nx = 2, max(1, seq_count // 32)
    nz = seq_count // (nx * cores)
    return nx, nz, cores


def solution(mesh):
    nx, nz, nc = split_seq(mesh)
    parts = {"seq": ((nx, nz, nc), ("sx", "sz", "sc")), "grp": ((mesh.shape["grp"],), ("grp",))}
    shape = sum((parts[name][0] for name in mesh.axis_names), ())
    names = sum((parts[name][1] for name in mesh.axis_names), ())
    inner = Mesh(mesh.devices.reshape(shape), names)
    return jax.shard_map(
        on_device,
        mesh=inner,
        in_specs=(P(ROWS, None),) * 5,
        out_specs=(P(ROWS, None), P(ROWS, None)),
        check_vma=False,
    )
```

```python
import jax
import jax.numpy as jnp
import numpy as np
from jax import lax
from jax.sharding import Mesh
from jax.sharding import PartitionSpec as P

FEAT = 16
WINDOW = 256


PRECISE = lax.Precision.HIGHEST
HALF_ROOT = 0.7071067811865476
ROWS = ("grp", "sx", "sz", "sc")
LINK = jnp.bfloat16


def passed_along(block, axis, distance):
    devices = range(lax.axis_size(axis))
    route = [(i - distance, i) for i in devices if i - distance in devices]
    return lax.ppermute(block, axis, route)


def seq_index_of():
    return (
        lax.axis_index("sx") * (lax.axis_size("sz") * lax.axis_size("sc"))
        + lax.axis_index("sz") * lax.axis_size("sc")
        + lax.axis_index("sc")
    )


def pair_features(scaled):
    row_count, head_count, feat_count = scaled.shape
    columns = jnp.transpose(scaled, (1, 2, 0))
    lower_index, upper_index = np.triu_indices(feat_count)
    identity = np.eye(feat_count, dtype=np.float32)
    pick_lower = jnp.asarray(identity[:, lower_index])
    pick_upper = jnp.asarray(identity[:, upper_index])
    pair_weight = jnp.asarray(
        np.where(lower_index == upper_index, HALF_ROOT, 1.0).astype(np.float32)
    )
    left_side = jnp.einsum("hfr,fp->hpr", columns, pick_lower, precision=PRECISE)
    right_side = jnp.einsum("hfr,fp->hpr", columns, pick_upper, precision=PRECISE)
    paired = left_side * right_side * pair_weight[None, :, None]
    return jnp.concatenate(
        [jnp.ones((head_count, 1, row_count), jnp.float32), columns, paired], axis=1
    )


def prefix_before(local):
    chips = lax.axis_size("sx") * lax.axis_size("sz")
    core = lax.axis_index("sc")
    size = local.size
    unit = 2 * chips * 128
    padded = -(-size // unit) * unit
    width = padded // (2 * chips)
    flat = jnp.pad(local.reshape(-1), (0, padded - size)).reshape(2, chips, width)
    sent = jnp.where(core == 0, flat[1], flat[0])
    other = lax.ppermute(sent, "sc", [(0, 1), (1, 0)])
    mine = jnp.where(core == 0, flat[0], flat[1])
    chip_half = mine + other
    gathered = lax.all_to_all(chip_half.astype(LINK), ("sx", "sz"), 0, 0, tiled=True)
    gathered = gathered.astype(jnp.float32)
    before_chip = (jnp.cumsum(gathered, axis=0) - gathered).astype(LINK)
    chip_prefix = lax.all_to_all(before_chip, ("sx", "sz"), 0, 0, tiled=True)
    chip_prefix = chip_prefix.astype(jnp.float32)
    first_core = jnp.where(core == 0, flat[0], other)
    with_first = chip_prefix + first_core
    keep = jnp.where(core == 0, chip_prefix, with_first)
    give = jnp.where(core == 0, with_first, chip_prefix)
    got = lax.ppermute(give, "sc", [(0, 1), (1, 0)])
    halves = jnp.where(core == 0, jnp.stack([keep, got]), jnp.stack([got, keep]))
    return halves.reshape(-1)[:size].reshape(local.shape)


def on_device(linear_query, linear_key, values, window_query, window_key):
    row_count = values.shape[0]
    head_count = linear_query.shape[1] // FEAT
    value_width = values.shape[1] // head_count
    seq_index = seq_index_of()
    start_pos = seq_index * row_count
    query_scaled = (linear_query.astype(jnp.float32) * FEAT ** (-0.25)).reshape(
        row_count, head_count, FEAT
    )
    key_scaled = (linear_key.astype(jnp.float32) * FEAT ** (-0.25)).reshape(
        row_count, head_count, FEAT
    )
    value_heads = values.astype(jnp.float32).reshape(row_count, head_count, value_width)
    query_feats = pair_features(query_scaled)
    key_feats = pair_features(key_scaled)
    local_state = jnp.einsum("hpr,rhv->hpv", key_feats, value_heads, precision=PRECISE)
    local_norm = jnp.sum(key_feats, axis=2)
    local = jnp.concatenate([local_state, local_norm[:, :, None]], axis=2)
    prior = prefix_before(local)
    prior_state = prior[:, :, :value_width]
    prior_norm = prior[:, :, value_width]
    causal = jnp.arange(row_count)[:, None] >= jnp.arange(row_count)[None, :]
    inner_prod = jnp.einsum("thf,jhf->htj", query_scaled, key_scaled, precision=PRECISE)
    kernel = jnp.where(causal[None], 1.0 + inner_prod + 0.5 * inner_prod * inner_prod, 0.0)
    numerator = jnp.einsum("htj,jhv->thv", kernel, value_heads, precision=PRECISE) + jnp.einsum(
        "hpt,hpv->thv", query_feats, prior_state, precision=PRECISE
    )
    denominator = jnp.sum(kernel, axis=2).T + jnp.einsum(
        "hpt,hp->th", query_feats, prior_norm, precision=PRECISE
    )
    linear_out = (numerator / denominator[:, :, None]).reshape(row_count, head_count * value_width)
    seq_count = lax.axis_size("sx") * lax.axis_size("sz") * lax.axis_size("sc")
    span_rows = row_count
    reach_count = 2
    assert reach_count * row_count >= WINDOW
    flat_axes = ("sx", "sz", "sc")
    core = lax.axis_index("sc")
    route = [(i - 2, i) for i in range(2, seq_count)]
    far = lax.ppermute((window_key, values), flat_axes, route)
    near = lax.ppermute(
        jax.tree.map(lambda o, f: jnp.where(core == 0, o, f), (window_key, values), far),
        "sc",
        [(0, 1), (1, 0)],
    )
    moved_keys = [near[0], far[0]]
    moved_values = [near[1], far[1]]
    all_keys = jnp.concatenate(moved_keys[::-1] + [window_key], axis=0)
    all_values = jnp.concatenate(moved_values[::-1] + [values], axis=0)
    key_count = all_keys.shape[0]
    query_pos = start_pos + jnp.arange(row_count, dtype=jnp.int32)
    key_pos = start_pos - reach_count * span_rows + jnp.arange(key_count, dtype=jnp.int32)
    allowed = (
        (key_pos[None, :] <= query_pos[:, None])
        & (key_pos[None, :] > query_pos[:, None] - WINDOW)
        & (key_pos[None, :] >= 0)
    )
    scores = jnp.einsum(
        "thd,jhd->htj",
        window_query.reshape(row_count, head_count, value_width),
        all_keys.reshape(key_count, head_count, value_width),
        preferred_element_type=jnp.float32,
    ) * value_width ** (-0.5)
    masked = jnp.where(allowed[None], scores, -jnp.inf)
    largest = jnp.max(masked, axis=2, keepdims=True)
    exponent = jnp.exp(masked - largest)
    weights = (exponent / jnp.sum(exponent, axis=2, keepdims=True)).astype(jnp.bfloat16)
    mixed = jnp.einsum(
        "htj,jhv->thv",
        weights,
        all_values.reshape(key_count, head_count, value_width),
        preferred_element_type=jnp.float32,
    )
    window_out = mixed.astype(jnp.bfloat16).reshape(row_count, head_count * value_width)
    return (linear_out, window_out)


def split_seq(mesh):
    seq_devices = np.moveaxis(mesh.devices, mesh.axis_names.index("seq"), 0)[:, 0]
    seq_count = len(seq_devices)
    try:
        chips = sorted({tuple(d.coords) for d in seq_devices})
        cores = seq_count // len(chips)
        xs = sorted({c[0] for c in chips})
        nx = len(xs)
    except (AttributeError, TypeError):
        cores, nx = 2, max(1, seq_count // 32)
    nz = seq_count // (nx * cores)
    return nx, nz, cores


def solution(mesh):
    nx, nz, nc = split_seq(mesh)
    parts = {"seq": ((nx, nz, nc), ("sx", "sz", "sc")), "grp": ((mesh.shape["grp"],), ("grp",))}
    shape = sum((parts[name][0] for name in mesh.axis_names), ())
    names = sum((parts[name][1] for name in mesh.axis_names), ())
    inner = Mesh(mesh.devices.reshape(shape), names)
    return jax.shard_map(
        on_device,
        mesh=inner,
        in_specs=(P(ROWS, None),) * 5,
        out_specs=(P(ROWS, None), P(ROWS, None)),
        check_vma=False,
    )
```

```python
import jax
import jax.numpy as jnp
import numpy as np
from jax import lax
from jax.sharding import Mesh
from jax.sharding import PartitionSpec as P

FEAT = 16
WINDOW = 256


PRECISE = lax.Precision.HIGHEST
HALF_ROOT = 0.7071067811865476
ROWS = ("grp", "sx", "sz", "sc")
LINK = jnp.bfloat16


def passed_along(block, axis, distance):
    devices = range(lax.axis_size(axis))
    route = [(i - distance, i) for i in devices if i - distance in devices]
    return lax.ppermute(block, axis, route)


def seq_index_of():
    return (
        lax.axis_index("sx") * (lax.axis_size("sz") * lax.axis_size("sc"))
        + lax.axis_index("sz") * lax.axis_size("sc")
        + lax.axis_index("sc")
    )


def pair_features(scaled):
    row_count, head_count, feat_count = scaled.shape
    columns = jnp.transpose(scaled, (1, 2, 0))
    lower_index, upper_index = np.triu_indices(feat_count)
    identity = np.eye(feat_count, dtype=np.float32)
    pick_lower = jnp.asarray(identity[:, lower_index])
    pick_upper = jnp.asarray(identity[:, upper_index])
    pair_weight = jnp.asarray(
        np.where(lower_index == upper_index, HALF_ROOT, 1.0).astype(np.float32)
    )
    left_side = jnp.einsum("hfr,fp->hpr", columns, pick_lower, precision=PRECISE)
    right_side = jnp.einsum("hfr,fp->hpr", columns, pick_upper, precision=PRECISE)
    paired = left_side * right_side * pair_weight[None, :, None]
    return jnp.concatenate(
        [jnp.ones((head_count, 1, row_count), jnp.float32), columns, paired], axis=1
    )


def prefix_before(local, tied_before, tied_after):
    chips = lax.axis_size("sx") * lax.axis_size("sz")
    core = lax.axis_index("sc")
    size = local.size
    unit = 2 * chips * 128
    padded = -(-size // unit) * unit
    width = padded // (2 * chips)
    flat = jnp.pad(local.reshape(-1), (0, padded - size)).reshape(2, chips, width)
    sent = jnp.where(core == 0, flat[1], flat[0])
    other = lax.ppermute(sent, "sc", [(0, 1), (1, 0)])
    mine = jnp.where(core == 0, flat[0], flat[1])
    chip_half = mine + other
    outgoing, tied_before = lax.optimization_barrier((chip_half.astype(LINK), tied_before))
    gathered = lax.all_to_all(outgoing, ("sx", "sz"), 0, 0, tiled=True)
    gathered, tied_after = lax.optimization_barrier((gathered, tied_after))
    gathered = gathered.astype(jnp.float32)
    before_chip = (jnp.cumsum(gathered, axis=0) - gathered).astype(LINK)
    chip_prefix = lax.all_to_all(before_chip, ("sx", "sz"), 0, 0, tiled=True)
    chip_prefix = chip_prefix.astype(jnp.float32)
    first_core = jnp.where(core == 0, flat[0], other)
    with_first = chip_prefix + first_core
    keep = jnp.where(core == 0, chip_prefix, with_first)
    give = jnp.where(core == 0, with_first, chip_prefix)
    got = lax.ppermute(give, "sc", [(0, 1), (1, 0)])
    halves = jnp.where(core == 0, jnp.stack([keep, got]), jnp.stack([got, keep]))
    return halves.reshape(-1)[:size].reshape(local.shape), tied_before, tied_after


def on_device(linear_query, linear_key, values, window_query, window_key):
    row_count = values.shape[0]
    head_count = linear_query.shape[1] // FEAT
    value_width = values.shape[1] // head_count
    seq_index = seq_index_of()
    start_pos = seq_index * row_count
    query_scaled = (linear_query.astype(jnp.float32) * FEAT ** (-0.25)).reshape(
        row_count, head_count, FEAT
    )
    key_scaled = (linear_key.astype(jnp.float32) * FEAT ** (-0.25)).reshape(
        row_count, head_count, FEAT
    )
    value_heads = values.astype(jnp.float32).reshape(row_count, head_count, value_width)
    query_feats = pair_features(query_scaled)
    key_feats = pair_features(key_scaled)
    local_state = jnp.einsum("hpr,rhv->hpv", key_feats, value_heads, precision=PRECISE)
    local_norm = jnp.sum(key_feats, axis=2)
    local = jnp.concatenate([local_state, local_norm[:, :, None]], axis=2)
    seq_count = lax.axis_size("sx") * lax.axis_size("sz") * lax.axis_size("sc")
    prior, (window_key, values), window_query = prefix_before(
        local, (window_key, values), window_query
    )
    prior_state = prior[:, :, :value_width]
    prior_norm = prior[:, :, value_width]
    causal = jnp.arange(row_count)[:, None] >= jnp.arange(row_count)[None, :]
    inner_prod = jnp.einsum("thf,jhf->htj", query_scaled, key_scaled, precision=PRECISE)
    kernel = jnp.where(causal[None], 1.0 + inner_prod + 0.5 * inner_prod * inner_prod, 0.0)
    numerator = jnp.einsum("htj,jhv->thv", kernel, value_heads, precision=PRECISE) + jnp.einsum(
        "hpt,hpv->thv", query_feats, prior_state, precision=PRECISE
    )
    denominator = jnp.sum(kernel, axis=2).T + jnp.einsum(
        "hpt,hp->th", query_feats, prior_norm, precision=PRECISE
    )
    linear_out = (numerator / denominator[:, :, None]).reshape(row_count, head_count * value_width)
    span_rows = row_count
    reach_count = 2
    assert reach_count * row_count >= WINDOW
    flat_axes = ("sx", "sz", "sc")
    core = lax.axis_index("sc")
    route = [(i - 2, i) for i in range(2, seq_count)]
    far = lax.ppermute((window_key, values), flat_axes, route)
    near = lax.ppermute(
        jax.tree.map(lambda o, f: jnp.where(core == 0, o, f), (window_key, values), far),
        "sc",
        [(0, 1), (1, 0)],
    )
    moved_keys = [near[0], far[0]]
    moved_values = [near[1], far[1]]
    all_keys = jnp.concatenate(moved_keys[::-1] + [window_key], axis=0)
    all_values = jnp.concatenate(moved_values[::-1] + [values], axis=0)
    key_count = all_keys.shape[0]
    query_pos = start_pos + jnp.arange(row_count, dtype=jnp.int32)
    key_pos = start_pos - reach_count * span_rows + jnp.arange(key_count, dtype=jnp.int32)
    allowed = (
        (key_pos[None, :] <= query_pos[:, None])
        & (key_pos[None, :] > query_pos[:, None] - WINDOW)
        & (key_pos[None, :] >= 0)
    )
    scores = jnp.einsum(
        "thd,jhd->htj",
        window_query.reshape(row_count, head_count, value_width),
        all_keys.reshape(key_count, head_count, value_width),
        preferred_element_type=jnp.float32,
    ) * value_width ** (-0.5)
    masked = jnp.where(allowed[None], scores, -jnp.inf)
    largest = jnp.max(masked, axis=2, keepdims=True)
    exponent = jnp.exp(masked - largest)
    weights = (exponent / jnp.sum(exponent, axis=2, keepdims=True)).astype(jnp.bfloat16)
    mixed = jnp.einsum(
        "htj,jhv->thv",
        weights,
        all_values.reshape(key_count, head_count, value_width),
        preferred_element_type=jnp.float32,
    )
    window_out = mixed.astype(jnp.bfloat16).reshape(row_count, head_count * value_width)
    return (linear_out, window_out)


def split_seq(mesh):
    seq_devices = np.moveaxis(mesh.devices, mesh.axis_names.index("seq"), 0)[:, 0]
    seq_count = len(seq_devices)
    try:
        chips = sorted({tuple(d.coords) for d in seq_devices})
        cores = seq_count // len(chips)
        xs = sorted({c[0] for c in chips})
        nx = len(xs)
    except (AttributeError, TypeError):
        cores, nx = 2, max(1, seq_count // 32)
    nz = seq_count // (nx * cores)
    return nx, nz, cores


def solution(mesh):
    nx, nz, nc = split_seq(mesh)
    parts = {"seq": ((nx, nz, nc), ("sx", "sz", "sc")), "grp": ((mesh.shape["grp"],), ("grp",))}
    shape = sum((parts[name][0] for name in mesh.axis_names), ())
    names = sum((parts[name][1] for name in mesh.axis_names), ())
    inner = Mesh(mesh.devices.reshape(shape), names)
    return jax.shard_map(
        on_device,
        mesh=inner,
        in_specs=(P(ROWS, None),) * 5,
        out_specs=(P(ROWS, None), P(ROWS, None)),
        check_vma=False,
    )
```

```python
import jax
import jax.numpy as jnp
import numpy as np
from jax import lax
from jax.sharding import Mesh
from jax.sharding import PartitionSpec as P

FEAT = 16
WINDOW = 256


PRECISE = lax.Precision.HIGH
EXACT = lax.Precision.DEFAULT
HALF_ROOT = 0.7071067811865476
ROWS = ("grp", "sx", "sz", "sc")
LINK = jnp.bfloat16


def passed_along(block, axis, distance):
    devices = range(lax.axis_size(axis))
    route = [(i - distance, i) for i in devices if i - distance in devices]
    return lax.ppermute(block, axis, route)


def seq_index_of():
    return (
        lax.axis_index("sx") * (lax.axis_size("sz") * lax.axis_size("sc"))
        + lax.axis_index("sz") * lax.axis_size("sc")
        + lax.axis_index("sc")
    )


def pair_features(scaled):
    row_count, head_count, feat_count = scaled.shape
    columns = jnp.transpose(scaled, (1, 2, 0))
    lower_index, upper_index = np.triu_indices(feat_count)
    identity = np.eye(feat_count, dtype=np.float32)
    pick_lower = jnp.asarray(identity[:, lower_index])
    pick_upper = jnp.asarray(identity[:, upper_index])
    pair_weight = jnp.asarray(
        np.where(lower_index == upper_index, HALF_ROOT, 1.0).astype(np.float32)
    )
    left_side = jnp.einsum("hfr,fp->hpr", columns, pick_lower, precision=EXACT)
    right_side = jnp.einsum("hfr,fp->hpr", columns, pick_upper, precision=EXACT)
    paired = left_side * right_side * pair_weight[None, :, None]
    return jnp.concatenate(
        [jnp.ones((head_count, 1, row_count), jnp.float32), columns, paired], axis=1
    )


def prefix_before(local):
    chips = lax.axis_size("sx") * lax.axis_size("sz")
    core = lax.axis_index("sc")
    size = local.size
    unit = 2 * chips * 128
    padded = -(-size // unit) * unit
    width = padded // (2 * chips)
    flat = jnp.pad(local.reshape(-1), (0, padded - size)).reshape(2, chips, width)
    sent = jnp.where(core == 0, flat[1], flat[0])
    other = lax.ppermute(sent, "sc", [(0, 1), (1, 0)])
    mine = jnp.where(core == 0, flat[0], flat[1])
    chip_half = mine + other
    gathered = lax.all_to_all(chip_half.astype(LINK), ("sx", "sz"), 0, 0, tiled=True)
    gathered = gathered.astype(jnp.float32)
    before_chip = (jnp.cumsum(gathered, axis=0) - gathered).astype(LINK)
    chip_prefix = lax.all_to_all(before_chip, ("sx", "sz"), 0, 0, tiled=True)
    chip_prefix = chip_prefix.astype(jnp.float32)
    first_core = jnp.where(core == 0, flat[0], other)
    with_first = chip_prefix + first_core
    keep = jnp.where(core == 0, chip_prefix, with_first)
    give = jnp.where(core == 0, with_first, chip_prefix)
    got = lax.ppermute(give, "sc", [(0, 1), (1, 0)])
    halves = jnp.where(core == 0, jnp.stack([keep, got]), jnp.stack([got, keep]))
    return halves.reshape(-1)[:size].reshape(local.shape)


def on_device(linear_query, linear_key, values, window_query, window_key):
    row_count = values.shape[0]
    head_count = linear_query.shape[1] // FEAT
    value_width = values.shape[1] // head_count
    seq_index = seq_index_of()
    start_pos = seq_index * row_count
    query_scaled = (linear_query.astype(jnp.float32) * FEAT ** (-0.25)).reshape(
        row_count, head_count, FEAT
    )
    key_scaled = (linear_key.astype(jnp.float32) * FEAT ** (-0.25)).reshape(
        row_count, head_count, FEAT
    )
    value_heads = values.astype(jnp.float32).reshape(row_count, head_count, value_width)
    query_feats = pair_features(query_scaled)
    key_feats = pair_features(key_scaled)
    local_state = jnp.einsum("hpr,rhv->hpv", key_feats, value_heads, precision=PRECISE)
    local_norm = jnp.sum(key_feats, axis=2)
    local = jnp.concatenate([local_state, local_norm[:, :, None]], axis=2)
    prior = prefix_before(local)
    prior_state = prior[:, :, :value_width]
    prior_norm = prior[:, :, value_width]
    causal = jnp.arange(row_count)[:, None] >= jnp.arange(row_count)[None, :]
    inner_prod = jnp.einsum("thf,jhf->htj", query_scaled, key_scaled, precision=EXACT)
    kernel = jnp.where(causal[None], 1.0 + inner_prod + 0.5 * inner_prod * inner_prod, 0.0)
    numerator = jnp.einsum("htj,jhv->thv", kernel, value_heads, precision=PRECISE) + jnp.einsum(
        "hpt,hpv->thv", query_feats, prior_state, precision=PRECISE
    )
    denominator = jnp.sum(kernel, axis=2).T + jnp.einsum(
        "hpt,hp->th", query_feats, prior_norm, precision=PRECISE
    )
    linear_out = (numerator / denominator[:, :, None]).reshape(row_count, head_count * value_width)
    seq_count = lax.axis_size("sx") * lax.axis_size("sz") * lax.axis_size("sc")
    span_rows = row_count
    reach_count = 2
    assert reach_count * row_count >= WINDOW
    flat_axes = ("sx", "sz", "sc")
    core = lax.axis_index("sc")
    route = [(i - 2, i) for i in range(2, seq_count)]
    far = lax.ppermute((window_key, values), flat_axes, route)
    near = lax.ppermute(
        jax.tree.map(lambda o, f: jnp.where(core == 0, o, f), (window_key, values), far),
        "sc",
        [(0, 1), (1, 0)],
    )
    moved_keys = [near[0], far[0]]
    moved_values = [near[1], far[1]]
    all_keys = jnp.concatenate(moved_keys[::-1] + [window_key], axis=0)
    all_values = jnp.concatenate(moved_values[::-1] + [values], axis=0)
    key_count = all_keys.shape[0]
    query_pos = start_pos + jnp.arange(row_count, dtype=jnp.int32)
    key_pos = start_pos - reach_count * span_rows + jnp.arange(key_count, dtype=jnp.int32)
    allowed = (
        (key_pos[None, :] <= query_pos[:, None])
        & (key_pos[None, :] > query_pos[:, None] - WINDOW)
        & (key_pos[None, :] >= 0)
    )
    scores = jnp.einsum(
        "thd,jhd->htj",
        window_query.reshape(row_count, head_count, value_width),
        all_keys.reshape(key_count, head_count, value_width),
        preferred_element_type=jnp.float32,
    ) * value_width ** (-0.5)
    masked = jnp.where(allowed[None], scores, -jnp.inf)
    largest = jnp.max(masked, axis=2, keepdims=True)
    exponent = jnp.exp(masked - largest)
    weights = (exponent / jnp.sum(exponent, axis=2, keepdims=True)).astype(jnp.bfloat16)
    mixed = jnp.einsum(
        "htj,jhv->thv",
        weights,
        all_values.reshape(key_count, head_count, value_width),
        preferred_element_type=jnp.float32,
    )
    window_out = mixed.astype(jnp.bfloat16).reshape(row_count, head_count * value_width)
    return (linear_out, window_out)


def split_seq(mesh):
    seq_devices = np.moveaxis(mesh.devices, mesh.axis_names.index("seq"), 0)[:, 0]
    seq_count = len(seq_devices)
    try:
        chips = sorted({tuple(d.coords) for d in seq_devices})
        cores = seq_count // len(chips)
        xs = sorted({c[0] for c in chips})
        nx = len(xs)
    except (AttributeError, TypeError):
        cores, nx = 2, max(1, seq_count // 32)
    nz = seq_count // (nx * cores)
    return nx, nz, cores


def solution(mesh):
    nx, nz, nc = split_seq(mesh)
    parts = {"seq": ((nx, nz, nc), ("sx", "sz", "sc")), "grp": ((mesh.shape["grp"],), ("grp",))}
    shape = sum((parts[name][0] for name in mesh.axis_names), ())
    names = sum((parts[name][1] for name in mesh.axis_names), ())
    inner = Mesh(mesh.devices.reshape(shape), names)
    return jax.shard_map(
        on_device,
        mesh=inner,
        in_specs=(P(ROWS, None),) * 5,
        out_specs=(P(ROWS, None), P(ROWS, None)),
        check_vma=False,
    )
```

```python
import jax
import jax.numpy as jnp
import numpy as np
from jax import lax
from jax.sharding import Mesh
from jax.sharding import PartitionSpec as P

FEAT = 16
WINDOW = 256


PRECISE = lax.Precision.HIGH
EXACT = lax.Precision.DEFAULT
HALF_ROOT = 0.7071067811865476
ROWS = ("grp", "sx", "sz", "sc")
LINK = jnp.bfloat16


def passed_along(block, axis, distance):
    devices = range(lax.axis_size(axis))
    route = [(i - distance, i) for i in devices if i - distance in devices]
    return lax.ppermute(block, axis, route)


def seq_index_of():
    return (
        lax.axis_index("sx") * (lax.axis_size("sz") * lax.axis_size("sc"))
        + lax.axis_index("sz") * lax.axis_size("sc")
        + lax.axis_index("sc")
    )


def pair_features(scaled, rows):
    row_count, head_count, feat_count = scaled.shape
    columns = jnp.transpose(scaled, (1, 2, 0))
    lower_index, upper_index = np.triu_indices(feat_count)
    identity = np.eye(feat_count, dtype=np.float32)
    pick_lower = jnp.asarray(identity[:, lower_index])
    pick_upper = jnp.asarray(identity[:, upper_index])
    pair_weight = jnp.asarray(
        np.where(lower_index == upper_index, HALF_ROOT, 1.0).astype(np.float32)
    )
    left_side = jnp.einsum("hfr,fp->hpr", columns, pick_lower, precision=EXACT)
    right_side = jnp.einsum("hfr,fp->hpr", columns, pick_upper, precision=EXACT)
    paired = left_side * right_side * pair_weight[None, :, None]
    filler = rows - 1 - feat_count - paired.shape[1]
    return jnp.concatenate(
        [
            jnp.ones((head_count, 1, row_count), jnp.float32),
            columns,
            paired,
            jnp.zeros((head_count, filler, row_count), jnp.float32),
        ],
        axis=1,
    )


def prefix_before(local):
    chips = lax.axis_size("sx") * lax.axis_size("sz")
    core = lax.axis_index("sc")
    size = local.size
    unit = 2 * chips * 128
    padded = -(-size // unit) * unit
    width = padded // (2 * chips)
    flat = jnp.pad(local.reshape(-1), (0, padded - size)).reshape(2, chips, width)
    sent = jnp.where(core == 0, flat[1], flat[0])
    other = lax.ppermute(sent, "sc", [(0, 1), (1, 0)])
    mine = jnp.where(core == 0, flat[0], flat[1])
    chip_half = mine + other
    gathered = lax.all_to_all(chip_half.astype(LINK), ("sx", "sz"), 0, 0, tiled=True)
    gathered = gathered.astype(jnp.float32)
    before_chip = (jnp.cumsum(gathered, axis=0) - gathered).astype(LINK)
    chip_prefix = lax.all_to_all(before_chip, ("sx", "sz"), 0, 0, tiled=True)
    chip_prefix = chip_prefix.astype(jnp.float32)
    first_core = jnp.where(core == 0, flat[0], other)
    with_first = chip_prefix + first_core
    keep = jnp.where(core == 0, chip_prefix, with_first)
    give = jnp.where(core == 0, with_first, chip_prefix)
    got = lax.ppermute(give, "sc", [(0, 1), (1, 0)])
    halves = jnp.where(core == 0, jnp.stack([keep, got]), jnp.stack([got, keep]))
    return halves.reshape(-1)[:size].reshape(local.shape)


def on_device(linear_query, linear_key, values, window_query, window_key):
    row_count = values.shape[0]
    head_count = linear_query.shape[1] // FEAT
    value_width = values.shape[1] // head_count
    seq_index = seq_index_of()
    start_pos = seq_index * row_count
    query_scaled = (linear_query.astype(jnp.float32) * FEAT ** (-0.25)).reshape(
        row_count, head_count, FEAT
    )
    key_scaled = (linear_key.astype(jnp.float32) * FEAT ** (-0.25)).reshape(
        row_count, head_count, FEAT
    )
    value_heads = values.astype(jnp.float32).reshape(row_count, head_count, value_width)
    feat_total = 1 + FEAT + FEAT * (FEAT + 1) // 2
    norm_rows = -(-feat_total // value_width)
    feat_rows = -(-(feat_total + norm_rows) // 8) * 8
    query_feats = pair_features(query_scaled, feat_rows)
    key_feats = pair_features(key_scaled, feat_rows)
    local_state = jnp.einsum("hpr,rhv->hpv", key_feats, value_heads, precision=PRECISE)
    local_norm = jnp.sum(key_feats[:, :feat_total], axis=2)
    norm_block = jnp.pad(local_norm, ((0, 0), (0, norm_rows * value_width - feat_total)))
    norm_block = norm_block.reshape(head_count, norm_rows, value_width)
    local = lax.dynamic_update_slice(local_state, norm_block, (0, feat_total, 0))
    prior = prefix_before(local)
    prior_state = prior
    prior_norm = prior[:, feat_total : feat_total + norm_rows].reshape(head_count, -1)[:, :feat_total]
    query_feats_only = query_feats[:, :feat_total]
    causal = jnp.arange(row_count)[:, None] >= jnp.arange(row_count)[None, :]
    inner_prod = jnp.einsum("thf,jhf->htj", query_scaled, key_scaled, precision=EXACT)
    kernel = jnp.where(causal[None], 1.0 + inner_prod + 0.5 * inner_prod * inner_prod, 0.0)
    numerator = jnp.einsum("htj,jhv->thv", kernel, value_heads, precision=PRECISE) + jnp.einsum(
        "hpt,hpv->thv", query_feats, prior_state, precision=PRECISE
    )
    denominator = jnp.sum(kernel, axis=2).T + jnp.einsum(
        "hpt,hp->th", query_feats_only, prior_norm, precision=PRECISE
    )
    linear_out = (numerator / denominator[:, :, None]).reshape(row_count, head_count * value_width)
    seq_count = lax.axis_size("sx") * lax.axis_size("sz") * lax.axis_size("sc")
    span_rows = row_count
    reach_count = 2
    assert reach_count * row_count >= WINDOW
    flat_axes = ("sx", "sz", "sc")
    core = lax.axis_index("sc")
    route = [(i - 2, i) for i in range(2, seq_count)]
    far = lax.ppermute((window_key, values), flat_axes, route)
    near = lax.ppermute(
        jax.tree.map(lambda o, f: jnp.where(core == 0, o, f), (window_key, values), far),
        "sc",
        [(0, 1), (1, 0)],
    )
    moved_keys = [near[0], far[0]]
    moved_values = [near[1], far[1]]
    all_keys = jnp.concatenate(moved_keys[::-1] + [window_key], axis=0)
    all_values = jnp.concatenate(moved_values[::-1] + [values], axis=0)
    key_count = all_keys.shape[0]
    query_pos = start_pos + jnp.arange(row_count, dtype=jnp.int32)
    key_pos = start_pos - reach_count * span_rows + jnp.arange(key_count, dtype=jnp.int32)
    allowed = (
        (key_pos[None, :] <= query_pos[:, None])
        & (key_pos[None, :] > query_pos[:, None] - WINDOW)
        & (key_pos[None, :] >= 0)
    )
    scores = jnp.einsum(
        "thd,jhd->htj",
        window_query.reshape(row_count, head_count, value_width),
        all_keys.reshape(key_count, head_count, value_width),
        preferred_element_type=jnp.float32,
    ) * value_width ** (-0.5)
    masked = jnp.where(allowed[None], scores, -jnp.inf)
    largest = jnp.max(masked, axis=2, keepdims=True)
    exponent = jnp.exp(masked - largest)
    weights = (exponent / jnp.sum(exponent, axis=2, keepdims=True)).astype(jnp.bfloat16)
    mixed = jnp.einsum(
        "htj,jhv->thv",
        weights,
        all_values.reshape(key_count, head_count, value_width),
        preferred_element_type=jnp.float32,
    )
    window_out = mixed.astype(jnp.bfloat16).reshape(row_count, head_count * value_width)
    return (linear_out, window_out)


def split_seq(mesh):
    seq_devices = np.moveaxis(mesh.devices, mesh.axis_names.index("seq"), 0)[:, 0]
    seq_count = len(seq_devices)
    try:
        chips = sorted({tuple(d.coords) for d in seq_devices})
        cores = seq_count // len(chips)
        xs = sorted({c[0] for c in chips})
        nx = len(xs)
    except (AttributeError, TypeError):
        cores, nx = 2, max(1, seq_count // 32)
    nz = seq_count // (nx * cores)
    return nx, nz, cores


def solution(mesh):
    nx, nz, nc = split_seq(mesh)
    parts = {"seq": ((nx, nz, nc), ("sx", "sz", "sc")), "grp": ((mesh.shape["grp"],), ("grp",))}
    shape = sum((parts[name][0] for name in mesh.axis_names), ())
    names = sum((parts[name][1] for name in mesh.axis_names), ())
    inner = Mesh(mesh.devices.reshape(shape), names)
    return jax.shard_map(
        on_device,
        mesh=inner,
        in_specs=(P(ROWS, None),) * 5,
        out_specs=(P(ROWS, None), P(ROWS, None)),
        check_vma=False,
    )
```

```python
import jax
import jax.numpy as jnp
import numpy as np
from jax import lax
from jax.sharding import Mesh
from jax.sharding import PartitionSpec as P

FEAT = 16
WINDOW = 256


PRECISE = lax.Precision.HIGH
EXACT = lax.Precision.DEFAULT
HALF_ROOT = 0.7071067811865476
ROWS = ("grp", "sx", "sz", "sc")
LINK = jnp.bfloat16


def passed_along(block, axis, distance):
    devices = range(lax.axis_size(axis))
    route = [(i - distance, i) for i in devices if i - distance in devices]
    return lax.ppermute(block, axis, route)


def seq_index_of():
    return (
        lax.axis_index("sx") * (lax.axis_size("sz") * lax.axis_size("sc"))
        + lax.axis_index("sz") * lax.axis_size("sc")
        + lax.axis_index("sc")
    )


def pair_features(scaled, rows):
    row_count, head_count, feat_count = scaled.shape
    columns = jnp.transpose(scaled, (1, 2, 0))
    lower_index, upper_index = np.triu_indices(feat_count)
    identity = np.eye(feat_count, dtype=np.float32)
    pick_lower = jnp.asarray(identity[:, lower_index])
    pick_upper = jnp.asarray(identity[:, upper_index])
    pair_weight = jnp.asarray(
        np.where(lower_index == upper_index, HALF_ROOT, 1.0).astype(np.float32)
    )
    left_side = jnp.einsum("hfr,fp->hpr", columns, pick_lower, precision=EXACT)
    right_side = jnp.einsum("hfr,fp->hpr", columns, pick_upper, precision=EXACT)
    paired = left_side * right_side * pair_weight[None, :, None]
    filler = rows - 1 - feat_count - paired.shape[1]
    return jnp.concatenate(
        [
            jnp.ones((head_count, 1, row_count), jnp.float32),
            columns,
            paired,
            jnp.zeros((head_count, filler, row_count), jnp.float32),
        ],
        axis=1,
    )


def prefix_before(local, tied):
    chips = lax.axis_size("sx") * lax.axis_size("sz")
    core = lax.axis_index("sc")
    size = local.size
    unit = 2 * chips * 128
    padded = -(-size // unit) * unit
    width = padded // (2 * chips)
    flat = jnp.pad(local.reshape(-1), (0, padded - size)).reshape(2, chips, width)
    sent = jnp.where(core == 0, flat[1], flat[0])
    other = lax.ppermute(sent, "sc", [(0, 1), (1, 0)])
    mine = jnp.where(core == 0, flat[0], flat[1])
    chip_half = mine + other
    outgoing, tied = lax.optimization_barrier((chip_half.astype(LINK), tied))
    gathered = lax.all_to_all(outgoing, ("sx", "sz"), 0, 0, tiled=True)
    gathered = gathered.astype(jnp.float32)
    before_chip = (jnp.cumsum(gathered, axis=0) - gathered).astype(LINK)
    chip_prefix = lax.all_to_all(before_chip, ("sx", "sz"), 0, 0, tiled=True)
    chip_prefix = chip_prefix.astype(jnp.float32)
    first_core = jnp.where(core == 0, flat[0], other)
    with_first = chip_prefix + first_core
    keep = jnp.where(core == 0, chip_prefix, with_first)
    give = jnp.where(core == 0, with_first, chip_prefix)
    got = lax.ppermute(give, "sc", [(0, 1), (1, 0)])
    halves = jnp.where(core == 0, jnp.stack([keep, got]), jnp.stack([got, keep]))
    return halves.reshape(-1)[:size].reshape(local.shape), tied


def on_device(linear_query, linear_key, values, window_query, window_key):
    row_count = values.shape[0]
    head_count = linear_query.shape[1] // FEAT
    value_width = values.shape[1] // head_count
    seq_index = seq_index_of()
    start_pos = seq_index * row_count
    query_scaled = (linear_query.astype(jnp.float32) * FEAT ** (-0.25)).reshape(
        row_count, head_count, FEAT
    )
    key_scaled = (linear_key.astype(jnp.float32) * FEAT ** (-0.25)).reshape(
        row_count, head_count, FEAT
    )
    value_heads = values.astype(jnp.float32).reshape(row_count, head_count, value_width)
    feat_total = 1 + FEAT + FEAT * (FEAT + 1) // 2
    norm_rows = -(-feat_total // value_width)
    feat_rows = -(-(feat_total + norm_rows) // 8) * 8
    query_feats = pair_features(query_scaled, feat_rows)
    key_feats = pair_features(key_scaled, feat_rows)
    local_state = jnp.einsum("hpr,rhv->hpv", key_feats, value_heads, precision=PRECISE)
    local_norm = jnp.sum(key_feats[:, :feat_total], axis=2)
    norm_block = jnp.pad(local_norm, ((0, 0), (0, norm_rows * value_width - feat_total)))
    norm_block = norm_block.reshape(head_count, norm_rows, value_width)
    local = lax.dynamic_update_slice(local_state, norm_block, (0, feat_total, 0))
    seq_count = lax.axis_size("sx") * lax.axis_size("sz") * lax.axis_size("sc")
    flat_axes = ("sx", "sz", "sc")
    route = [(i - 2, i) for i in range(2, seq_count)]
    far = lax.ppermute((window_key, values), flat_axes, route)
    prior, far = prefix_before(local, far)
    prior_state = prior
    prior_norm = prior[:, feat_total : feat_total + norm_rows].reshape(head_count, -1)[:, :feat_total]
    query_feats_only = query_feats[:, :feat_total]
    causal = jnp.arange(row_count)[:, None] >= jnp.arange(row_count)[None, :]
    inner_prod = jnp.einsum("thf,jhf->htj", query_scaled, key_scaled, precision=EXACT)
    kernel = jnp.where(causal[None], 1.0 + inner_prod + 0.5 * inner_prod * inner_prod, 0.0)
    numerator = jnp.einsum("htj,jhv->thv", kernel, value_heads, precision=PRECISE) + jnp.einsum(
        "hpt,hpv->thv", query_feats, prior_state, precision=PRECISE
    )
    denominator = jnp.sum(kernel, axis=2).T + jnp.einsum(
        "hpt,hp->th", query_feats_only, prior_norm, precision=PRECISE
    )
    linear_out = (numerator / denominator[:, :, None]).reshape(row_count, head_count * value_width)
    seq_count = lax.axis_size("sx") * lax.axis_size("sz") * lax.axis_size("sc")
    span_rows = row_count
    reach_count = 2
    assert reach_count * row_count >= WINDOW
    flat_axes = ("sx", "sz", "sc")
    core = lax.axis_index("sc")
    near = lax.ppermute(
        jax.tree.map(lambda o, f: jnp.where(core == 0, o, f), (window_key, values), far),
        "sc",
        [(0, 1), (1, 0)],
    )
    moved_keys = [near[0], far[0]]
    moved_values = [near[1], far[1]]
    all_keys = jnp.concatenate(moved_keys[::-1] + [window_key], axis=0)
    all_values = jnp.concatenate(moved_values[::-1] + [values], axis=0)
    key_count = all_keys.shape[0]
    query_pos = start_pos + jnp.arange(row_count, dtype=jnp.int32)
    key_pos = start_pos - reach_count * span_rows + jnp.arange(key_count, dtype=jnp.int32)
    allowed = (
        (key_pos[None, :] <= query_pos[:, None])
        & (key_pos[None, :] > query_pos[:, None] - WINDOW)
        & (key_pos[None, :] >= 0)
    )
    scores = jnp.einsum(
        "thd,jhd->htj",
        window_query.reshape(row_count, head_count, value_width),
        all_keys.reshape(key_count, head_count, value_width),
        preferred_element_type=jnp.float32,
    ) * value_width ** (-0.5)
    masked = jnp.where(allowed[None], scores, -jnp.inf)
    largest = jnp.max(masked, axis=2, keepdims=True)
    exponent = jnp.exp(masked - largest)
    weights = (exponent / jnp.sum(exponent, axis=2, keepdims=True)).astype(jnp.bfloat16)
    mixed = jnp.einsum(
        "htj,jhv->thv",
        weights,
        all_values.reshape(key_count, head_count, value_width),
        preferred_element_type=jnp.float32,
    )
    window_out = mixed.astype(jnp.bfloat16).reshape(row_count, head_count * value_width)
    return (linear_out, window_out)


def split_seq(mesh):
    seq_devices = np.moveaxis(mesh.devices, mesh.axis_names.index("seq"), 0)[:, 0]
    seq_count = len(seq_devices)
    try:
        chips = sorted({tuple(d.coords) for d in seq_devices})
        cores = seq_count // len(chips)
        xs = sorted({c[0] for c in chips})
        nx = len(xs)
    except (AttributeError, TypeError):
        cores, nx = 2, max(1, seq_count // 32)
    nz = seq_count // (nx * cores)
    return nx, nz, cores


def solution(mesh):
    nx, nz, nc = split_seq(mesh)
    parts = {"seq": ((nx, nz, nc), ("sx", "sz", "sc")), "grp": ((mesh.shape["grp"],), ("grp",))}
    shape = sum((parts[name][0] for name in mesh.axis_names), ())
    names = sum((parts[name][1] for name in mesh.axis_names), ())
    inner = Mesh(mesh.devices.reshape(shape), names)
    return jax.shard_map(
        on_device,
        mesh=inner,
        in_specs=(P(ROWS, None),) * 5,
        out_specs=(P(ROWS, None), P(ROWS, None)),
        check_vma=False,
    )
```

```python
import jax
import jax.numpy as jnp
import numpy as np
from jax import lax
from jax.sharding import Mesh
from jax.sharding import PartitionSpec as P

FEAT = 16
WINDOW = 256


PRECISE = lax.Precision.HIGH
EXACT = lax.Precision.DEFAULT
HALF_ROOT = 0.7071067811865476
ROWS = ("grp", "sx", "sz", "sc")
LINK = jnp.bfloat16


def passed_along(block, axis, distance):
    devices = range(lax.axis_size(axis))
    route = [(i - distance, i) for i in devices if i - distance in devices]
    return lax.ppermute(block, axis, route)


def seq_index_of():
    return (
        lax.axis_index("sx") * (lax.axis_size("sz") * lax.axis_size("sc"))
        + lax.axis_index("sz") * lax.axis_size("sc")
        + lax.axis_index("sc")
    )


def pair_features(scaled, rows):
    row_count, head_count, feat_count = scaled.shape
    columns = jnp.transpose(scaled, (1, 2, 0))
    lower_index, upper_index = np.triu_indices(feat_count)
    identity = np.eye(feat_count, dtype=np.float32)
    pick_lower = jnp.asarray(identity[:, lower_index])
    pick_upper = jnp.asarray(identity[:, upper_index])
    pair_weight = jnp.asarray(
        np.where(lower_index == upper_index, HALF_ROOT, 1.0).astype(np.float32)
    )
    left_side = jnp.einsum("hfr,fp->hpr", columns, pick_lower, precision=EXACT)
    right_side = jnp.einsum("hfr,fp->hpr", columns, pick_upper, precision=EXACT)
    paired = left_side * right_side * pair_weight[None, :, None]
    filler = rows - 1 - feat_count - paired.shape[1]
    return jnp.concatenate(
        [
            jnp.ones((head_count, 1, row_count), jnp.float32),
            columns,
            paired,
            jnp.zeros((head_count, filler, row_count), jnp.float32),
        ],
        axis=1,
    )


def prefix_before(local, tied, settle):
    chips = lax.axis_size("sx") * lax.axis_size("sz")
    core = lax.axis_index("sc")
    size = local.size
    unit = 2 * chips * 128
    padded = -(-size // unit) * unit
    width = padded // (2 * chips)
    flat = jnp.pad(local.reshape(-1), (0, padded - size)).reshape(2, chips, width)
    sent = jnp.where(core == 0, flat[1], flat[0])
    other = lax.ppermute(sent, "sc", [(0, 1), (1, 0)])
    mine = jnp.where(core == 0, flat[0], flat[1])
    chip_half = mine + other
    outgoing, tied = lax.optimization_barrier((chip_half.astype(LINK), tied))
    gathered = lax.all_to_all(outgoing, ("sx", "sz"), 0, 0, tiled=True)
    gathered, settled = lax.optimization_barrier((gathered, settle(tied)))
    gathered = gathered.astype(jnp.float32)
    before_chip = (jnp.cumsum(gathered, axis=0) - gathered).astype(LINK)
    chip_prefix = lax.all_to_all(before_chip, ("sx", "sz"), 0, 0, tiled=True)
    chip_prefix = chip_prefix.astype(jnp.float32)
    first_core = jnp.where(core == 0, flat[0], other)
    with_first = chip_prefix + first_core
    keep = jnp.where(core == 0, chip_prefix, with_first)
    give = jnp.where(core == 0, with_first, chip_prefix)
    got = lax.ppermute(give, "sc", [(0, 1), (1, 0)])
    halves = jnp.where(core == 0, jnp.stack([keep, got]), jnp.stack([got, keep]))
    return halves.reshape(-1)[:size].reshape(local.shape), tied, settled


def on_device(linear_query, linear_key, values, window_query, window_key):
    row_count = values.shape[0]
    head_count = linear_query.shape[1] // FEAT
    value_width = values.shape[1] // head_count
    seq_index = seq_index_of()
    start_pos = seq_index * row_count
    query_scaled = (linear_query.astype(jnp.float32) * FEAT ** (-0.25)).reshape(
        row_count, head_count, FEAT
    )
    key_scaled = (linear_key.astype(jnp.float32) * FEAT ** (-0.25)).reshape(
        row_count, head_count, FEAT
    )
    value_heads = values.astype(jnp.float32).reshape(row_count, head_count, value_width)
    feat_total = 1 + FEAT + FEAT * (FEAT + 1) // 2
    norm_rows = -(-feat_total // value_width)
    feat_rows = -(-(feat_total + norm_rows) // 8) * 8
    query_feats = pair_features(query_scaled, feat_rows)
    key_feats = pair_features(key_scaled, feat_rows)
    local_state = jnp.einsum("hpr,rhv->hpv", key_feats, value_heads, precision=PRECISE)
    local_norm = jnp.sum(key_feats[:, :feat_total], axis=2)
    norm_block = jnp.pad(local_norm, ((0, 0), (0, norm_rows * value_width - feat_total)))
    norm_block = norm_block.reshape(head_count, norm_rows, value_width)
    local = lax.dynamic_update_slice(local_state, norm_block, (0, feat_total, 0))
    seq_count = lax.axis_size("sx") * lax.axis_size("sz") * lax.axis_size("sc")
    flat_axes = ("sx", "sz", "sc")
    route = [(i - 2, i) for i in range(2, seq_count)]
    far = lax.ppermute((window_key, values), flat_axes, route)
    core = lax.axis_index("sc")

    def near_of(far):
        return lax.ppermute(
            jax.tree.map(lambda o, f: jnp.where(core == 0, o, f), (window_key, values), far),
            "sc",
            [(0, 1), (1, 0)],
        )

    prior, far, near = prefix_before(local, far, near_of)
    prior_state = prior
    prior_norm = prior[:, feat_total : feat_total + norm_rows].reshape(head_count, -1)[:, :feat_total]
    query_feats_only = query_feats[:, :feat_total]
    causal = jnp.arange(row_count)[:, None] >= jnp.arange(row_count)[None, :]
    inner_prod = jnp.einsum("thf,jhf->htj", query_scaled, key_scaled, precision=EXACT)
    kernel = jnp.where(causal[None], 1.0 + inner_prod + 0.5 * inner_prod * inner_prod, 0.0)
    numerator = jnp.einsum("htj,jhv->thv", kernel, value_heads, precision=PRECISE) + jnp.einsum(
        "hpt,hpv->thv", query_feats, prior_state, precision=PRECISE
    )
    denominator = jnp.sum(kernel, axis=2).T + jnp.einsum(
        "hpt,hp->th", query_feats_only, prior_norm, precision=PRECISE
    )
    linear_out = (numerator / denominator[:, :, None]).reshape(row_count, head_count * value_width)
    seq_count = lax.axis_size("sx") * lax.axis_size("sz") * lax.axis_size("sc")
    span_rows = row_count
    reach_count = 2
    assert reach_count * row_count >= WINDOW
    flat_axes = ("sx", "sz", "sc")
    core = lax.axis_index("sc")
    moved_keys = [near[0], far[0]]
    moved_values = [near[1], far[1]]
    all_keys = jnp.concatenate(moved_keys[::-1] + [window_key], axis=0)
    all_values = jnp.concatenate(moved_values[::-1] + [values], axis=0)
    key_count = all_keys.shape[0]
    query_pos = start_pos + jnp.arange(row_count, dtype=jnp.int32)
    key_pos = start_pos - reach_count * span_rows + jnp.arange(key_count, dtype=jnp.int32)
    allowed = (
        (key_pos[None, :] <= query_pos[:, None])
        & (key_pos[None, :] > query_pos[:, None] - WINDOW)
        & (key_pos[None, :] >= 0)
    )
    scores = jnp.einsum(
        "thd,jhd->htj",
        window_query.reshape(row_count, head_count, value_width),
        all_keys.reshape(key_count, head_count, value_width),
        preferred_element_type=jnp.float32,
    ) * value_width ** (-0.5)
    masked = jnp.where(allowed[None], scores, -jnp.inf)
    largest = jnp.max(masked, axis=2, keepdims=True)
    exponent = jnp.exp(masked - largest)
    weights = (exponent / jnp.sum(exponent, axis=2, keepdims=True)).astype(jnp.bfloat16)
    mixed = jnp.einsum(
        "htj,jhv->thv",
        weights,
        all_values.reshape(key_count, head_count, value_width),
        preferred_element_type=jnp.float32,
    )
    window_out = mixed.astype(jnp.bfloat16).reshape(row_count, head_count * value_width)
    return (linear_out, window_out)


def split_seq(mesh):
    seq_devices = np.moveaxis(mesh.devices, mesh.axis_names.index("seq"), 0)[:, 0]
    seq_count = len(seq_devices)
    try:
        chips = sorted({tuple(d.coords) for d in seq_devices})
        cores = seq_count // len(chips)
        xs = sorted({c[0] for c in chips})
        nx = len(xs)
    except (AttributeError, TypeError):
        cores, nx = 2, max(1, seq_count // 32)
    nz = seq_count // (nx * cores)
    return nx, nz, cores


def solution(mesh):
    nx, nz, nc = split_seq(mesh)
    parts = {"seq": ((nx, nz, nc), ("sx", "sz", "sc")), "grp": ((mesh.shape["grp"],), ("grp",))}
    shape = sum((parts[name][0] for name in mesh.axis_names), ())
    names = sum((parts[name][1] for name in mesh.axis_names), ())
    inner = Mesh(mesh.devices.reshape(shape), names)
    return jax.shard_map(
        on_device,
        mesh=inner,
        in_specs=(P(ROWS, None),) * 5,
        out_specs=(P(ROWS, None), P(ROWS, None)),
        check_vma=False,
    )
```
